256 devices in a mesh: row: 16 (over x, y_lo, core), col: 16 (over y_hi, z).
Axes of the slice: x: 4, y: 4 (y_hi: 2, y_lo: 2; y = y_hi * 2 + y_lo), z: 8, core: 2. Of those that a mesh axis runs over, the one named last changes fastest.
Arguments:
- coeffs: bfloat16 [4096, 4096], P('row', 'col'), may hold values from -6 to 6
- block_tiles: bfloat16 [64, 48, 64, 64], P('col', 'row'), may hold values from -0.15625 to 0.15625
- neighbours: int32 [64, 48], P('col'), may hold values from 0 to 63, as said below
- density: int32 [32], replicated, may hold values from 6 to 48, as said below
Outputs:
- filtered: bfloat16 [4096, 4096], P('row', 'col')
The draws below stay inside these ranges and needn't reach their ends.
Inputs may be any that keep to these rules, and one draw needn't show every extreme that they name: `neighbours`: slot 0 of block row b holds b itself. Where 48 <= 64 the slots of one block row name distinct block rows; otherwise every block row is named in each row and some more than once, whose tiles then add. `density`: the number of leading live slots of every block row of a region; some region has 48 and some has 6 in every draw.
All inputs are finite; a program needn't handle non-finite values.
Results may differ from the reference program's by a relative error of at most 0.0054.
Values may be sent and summed in bfloat16 or wider, within the bound.
No kernel may reach another device: no remote copies, remote signals or barrier semaphores. Data moves between devices by JAX's collectives and lax.ppermute only.
A program may use at most 64 MiB of HBM per device.

```python
import jax
import jax.numpy as jnp
from jax import lax

M = 4096
BS = 64
K = 48
STEPS = 3
REG_BLK = 2
NB = 64
N = 4096
REGIONS = 32


def draw_neighbours(key, part):
    row_keys = jax.random.split(key, NB)

    def one_order(row_key):
        return jax.random.permutation(row_key, NB - 1).astype(jnp.int32)
    orders = jax.vmap(one_order)(row_keys)
    repeats = (K - 1) // (NB - 1) + 1
    offsets = jnp.tile(orders, (1, repeats))[:, :K - 1] + 1
    own_block = jnp.arange(NB, dtype=jnp.int32)
    others = (own_block[:, None] + offsets) % NB
    return jnp.concatenate([own_block[:, None], others.astype(jnp.int32)], axis=1)


def draw_density(key, part):
    key_level = jax.random.fold_in(key, 11)
    key_high = jax.random.fold_in(key, 23)
    key_low = jax.random.fold_in(key, 37)
    levels = jax.random.randint(key_level, (REGIONS,), K // 8, K + 1, dtype=jnp.int32)
    highest = jax.random.randint(key_high, (), 0, REGIONS, dtype=jnp.int32)
    offset = jax.random.randint(key_low, (), 1, REGIONS, dtype=jnp.int32)
    lowest = (highest + offset) % REGIONS
    return levels.at[highest].set(K).at[lowest].set(K // 8)


def level_of(key, extent, shards, least, top_value):
    loudness = 1.0
    for position, shards_of in shards:
        heights = jax.random.uniform(jax.random.fold_in(jax.random.fold_in(key, 6), position), (shards_of,), jnp.float32, least / len(shards), top_value / len(shards))
        loudness = loudness * jnp.repeat(jnp.exp(heights), extent[position] // shards_of).reshape((-1,) + (1,) * (len(extent) - 1 - position))
    return loudness


def centred(key, extent, scale, limit, pieces=(), kind=jnp.bfloat16):
    level = level_of(key, extent, pieces, -0.22, 0.18) if pieces else 1.0
    array = jax.random.normal(key, extent, jnp.float32) * scale * level
    return jnp.minimum(jnp.maximum(array, -limit), limit).astype(kind)


def setup_inputs(seed: int = 0) -> dict:
    seeds = jax.random.split(jax.random.key(seed), 5)
    return {
        "coeffs": centred(seeds[0], (M, N), 1.0, 6.0, ((0, 16), (1, 16))),
        "block_tiles": centred(seeds[1], (NB, K, BS, BS), (K * BS // 2) ** -0.5, 0.15625, ((0, 16), (1, 16))),
        "neighbours": draw_neighbours(jax.random.fold_in(seeds[4], 71), 0),
        "density": draw_density(jax.random.fold_in(seeds[4], 71), 0),
    }


def live_slots(density):
    block_ids = jnp.arange(NB, dtype=jnp.int32)
    live_counts = density[block_ids // REG_BLK]
    return jnp.arange(K, dtype=jnp.int32)[None, :] < live_counts[:, None]


def apply_hamiltonian(block_tiles, neighbours, live_mask, coefficients):
    blocks = coefficients.astype(jnp.float32).reshape(M, NB, BS)

    def block_row(row_inputs):
        row_tiles, row_neighbours, row_live = row_inputs
        gathered = jnp.take(blocks, row_neighbours, axis=1)
        masked = jnp.where(row_live[:, None, None], row_tiles.astype(jnp.float32), 0.0)
        return jnp.einsum("msj,sij->mi", gathered, masked, precision=lax.Precision.HIGHEST)

    row_results = lax.map(block_row, (block_tiles, neighbours, live_mask))
    return jnp.transpose(row_results, (1, 0, 2)).reshape(M, N)


def reference(coeffs, block_tiles, neighbours, density):
    live_mask = live_slots(density)
    previous = coeffs
    current = apply_hamiltonian(block_tiles, neighbours, live_mask, coeffs).astype(jnp.bfloat16)
    for repeat in range(STEPS - 1):
        product = apply_hamiltonian(block_tiles, neighbours, live_mask, current)
        following = (2.0 * product - previous.astype(jnp.float32)).astype(jnp.bfloat16)
        previous = current
        current = following
    return current
```

```python
import jax
import jax.numpy as jnp
from jax import lax
from jax.sharding import Mesh, PartitionSpec as P

STEPS = 3
REG_BLK = 2

ROW_AXES = ("x", "y_lo", "core")
COL_AXES = ("y_hi", "z")


def gather_col(field, y_count, z_count):
    y = lax.axis_index("y_hi")
    pairs = [field]
    for shift in range(1, y_count):
        pairs.append(lax.ppermute(field, "y_hi", [(i, (i + shift) % y_count) for i in range(y_count)]))
    pair = jnp.roll(jnp.stack(pairs)[::-1], y + 1, axis=0)
    fwd = [(i, (i + 1) % z_count) for i in range(z_count)]
    bwd = [(i, (i - 1) % z_count) for i in range(z_count)]
    blocks = [None] * z_count
    blocks[0] = pair
    right = pair
    left = pair
    half = z_count // 2
    for k in range(1, (z_count + 1) // 2):
        right = lax.ppermute(right, "z", fwd)
        left = lax.ppermute(left, "z", bwd)
        blocks[(-k) % z_count] = right
        blocks[k] = left
    if z_count % 2 == 0 and z_count > 1:
        split = y_count // 2
        if split == 0:
            blocks[half] = lax.ppermute(right, "z", fwd)
        else:
            lo = lax.ppermute(right[:split], "z", fwd)
            hi = lax.ppermute(left[split:], "z", bwd)
            blocks[half] = jnp.concatenate([lo, hi], axis=0)
    return blocks


def body(coeffs, block_tiles, neighbours, density):
    y_count = lax.axis_size("y_hi")
    z_count = lax.axis_size("z")
    local_width = coeffs.shape[1]
    block_rows = neighbours.shape[0]
    slot_count = neighbours.shape[1]
    block_size = block_tiles.shape[2]
    total_blocks = block_rows * y_count * z_count
    col = lax.axis_index("y_hi") * z_count + lax.axis_index("z")
    block_ids = col * block_rows + jnp.arange(block_rows, dtype=jnp.int32)
    region_ids = block_ids // REG_BLK
    region_match = region_ids[:, None] == jnp.arange(density.shape[0], dtype=jnp.int32)[None, :]
    live_counts = jnp.sum(jnp.where(region_match, density[None, :], 0), axis=1)
    live_mask = jnp.arange(slot_count, dtype=jnp.int32)[None, :] < live_counts[:, None]

    tiles = lax.all_gather(block_tiles, ROW_AXES, axis=1, tiled=True)
    pick = (neighbours[:, :, None] == jnp.arange(total_blocks, dtype=jnp.int32)[None, None, :]) & live_mask[:, :, None]
    dense = jnp.einsum("bsn,bsij->njbi", pick.astype(tiles.dtype), tiles, preferred_element_type=jnp.float32)
    dense = dense.astype(tiles.dtype).reshape(y_count, z_count, local_width, local_width)
    dense = jnp.roll(dense, -lax.axis_index("z"), axis=1)

    def apply_hamiltonian(field):
        blocks = gather_col(field, y_count, z_count)
        total = None
        for d, chunk in enumerate(blocks):
            part = jnp.einsum("ymj,yjo->mo", chunk, dense[:, d], preferred_element_type=jnp.float32)
            total = part if total is None else total + part
        return total

    previous = coeffs
    current = apply_hamiltonian(coeffs).astype(jnp.bfloat16)
    for repeat in range(STEPS - 1):
        product = apply_hamiltonian(current)
        following = (2.0 * product - previous.astype(jnp.float32)).astype(jnp.bfloat16)
        previous = current
        current = following
    return current


def solution(mesh):
    devices = mesh.devices.reshape(4, 2, 2, 2, 8)
    fine = Mesh(devices, ROW_AXES + COL_AXES)
    placed = (P(ROW_AXES, COL_AXES), P(COL_AXES, ROW_AXES, None, None), P(COL_AXES, None), P())
    return jax.shard_map(
        body, mesh=fine, in_specs=placed, out_specs=P(ROW_AXES, COL_AXES), check_vma=False
    )
```

```python
import jax
import jax.numpy as jnp
from jax import lax
from jax.sharding import Mesh, PartitionSpec as P

STEPS = 3
REG_BLK = 2

ROW_AXES = ("x", "y_lo", "core")
COL_AXES = ("y_hi", "z")


def ring_blocks(piece, axis, count, split_dim):
    fwd = [(i, (i + 1) % count) for i in range(count)]
    bwd = [(i, (i - 1) % count) for i in range(count)]
    blocks = [None] * count
    blocks[0] = piece
    right = piece
    left = piece
    for k in range(1, (count + 1) // 2):
        right = lax.ppermute(right, axis, fwd)
        left = lax.ppermute(left, axis, bwd)
        blocks[(-k) % count] = right
        blocks[k] = left
    if count % 2 == 0 and count > 1:
        if count == 2:
            blocks[1] = lax.ppermute(piece, axis, fwd)
        else:
            split = piece.shape[split_dim] // 2
            lo = lax.ppermute(lax.slice_in_dim(right, 0, split, axis=split_dim), axis, fwd)
            hi = lax.ppermute(lax.slice_in_dim(left, split, None, axis=split_dim), axis, bwd)
            blocks[count // 2] = jnp.concatenate([lo, hi], axis=split_dim)
    return blocks


def in_order(blocks, axis):
    return jnp.roll(jnp.stack(blocks), lax.axis_index(axis), axis=0)


def gather_col(field, y_count, z_count):
    pair = in_order(ring_blocks(field, "y_hi", y_count, 0), "y_hi")
    return ring_blocks(pair, "z", z_count, 0)


def gather_slots(tiles):
    local_slots = tiles.shape[1]
    slot_map = jnp.arange(local_slots, dtype=jnp.int32)
    stride = 1
    for axis in ROW_AXES[::-1]:
        count = lax.axis_size(axis)
        stacked = jnp.stack(ring_blocks(tiles, axis, count, 0))
        tiles = jnp.moveaxis(stacked, 0, 1).reshape(tiles.shape[0], -1, *tiles.shape[2:])
        owner = (lax.axis_index(axis) + jnp.arange(count, dtype=jnp.int32)) % count
        slot_map = (owner[:, None] * (stride * local_slots) + slot_map[None, :]).reshape(-1)
        stride = stride * count
    return tiles, slot_map


def body(coeffs, block_tiles, neighbours, density):
    y_count = lax.axis_size("y_hi")
    z_count = lax.axis_size("z")
    local_width = coeffs.shape[1]
    block_rows = neighbours.shape[0]
    slot_count = neighbours.shape[1]
    block_size = block_tiles.shape[2]
    total_blocks = block_rows * y_count * z_count
    col = lax.axis_index("y_hi") * z_count + lax.axis_index("z")
    block_ids = col * block_rows + jnp.arange(block_rows, dtype=jnp.int32)
    region_ids = block_ids // REG_BLK
    region_match = region_ids[:, None] == jnp.arange(density.shape[0], dtype=jnp.int32)[None, :]
    live_counts = jnp.sum(jnp.where(region_match, density[None, :], 0), axis=1)
    live_mask = jnp.arange(slot_count, dtype=jnp.int32)[None, :] < live_counts[:, None]

    tiles, slot_map = gather_slots(block_tiles)
    ring_neighbours = neighbours[:, slot_map]
    ring_live = live_mask[:, slot_map]
    rows = jnp.arange(total_blocks, dtype=jnp.int32)
    per_col = block_rows
    row_y = rows // (z_count * per_col)
    row_d = (rows // per_col) % z_count
    row_block = (row_y * z_count + (row_d + lax.axis_index("z")) % z_count) * per_col + rows % per_col
    pick = (ring_neighbours[:, :, None] == row_block[None, None, :]) & ring_live[:, :, None]
    dense = jnp.einsum("bsn,bsij->njbi", pick.astype(tiles.dtype), tiles, preferred_element_type=tiles.dtype)
    dense = dense.reshape(y_count, z_count, local_width, local_width)

    def apply_hamiltonian(field):
        blocks = gather_col(field, y_count, z_count)
        total = None
        for d, chunk in enumerate(blocks):
            part = jnp.einsum("ymj,yjo->mo", chunk, dense[:, d], preferred_element_type=jnp.float32)
            total = part if total is None else total + part
        return total

    previous = coeffs
    current = apply_hamiltonian(coeffs).astype(jnp.bfloat16)

    def recurse(repeat, carry):
        previous, current = carry
        product = apply_hamiltonian(current)
        following = (2.0 * product - previous.astype(jnp.float32)).astype(jnp.bfloat16)
        return current, following

    previous, current = lax.fori_loop(0, STEPS - 1, recurse, (previous, current))
    return current


def solution(mesh):
    devices = mesh.devices.reshape(4, 2, 2, 2, 8)
    fine = Mesh(devices, ROW_AXES + COL_AXES)
    placed = (P(ROW_AXES, COL_AXES), P(COL_AXES, ROW_AXES, None, None), P(COL_AXES, None), P())
    return jax.shard_map(
        body, mesh=fine, in_specs=placed, out_specs=P(ROW_AXES, COL_AXES), check_vma=False
    )
```

```python
import jax
import jax.numpy as jnp
from jax import lax
from jax.experimental import pallas as pl
from jax.experimental.pallas import tpu as pltpu
from jax.sharding import Mesh, PartitionSpec as P

STEPS = 3
REG_BLK = 2

ROW_AXES = ("x", "y_lo", "core")
COL_AXES = ("y_hi", "z")


def ring_blocks(piece, axis, count, split_dim):
    fwd = [(i, (i + 1) % count) for i in range(count)]
    bwd = [(i, (i - 1) % count) for i in range(count)]
    blocks = [None] * count
    blocks[0] = piece
    right = piece
    left = piece
    for k in range(1, (count + 1) // 2):
        right = lax.ppermute(right, axis, fwd)
        left = lax.ppermute(left, axis, bwd)
        blocks[(-k) % count] = right
        blocks[k] = left
    if count % 2 == 0 and count > 1:
        if count == 2:
            blocks[1] = lax.ppermute(piece, axis, fwd)
        else:
            split = piece.shape[split_dim] // 2
            lo = lax.ppermute(lax.slice_in_dim(right, 0, split, axis=split_dim), axis, fwd)
            hi = lax.ppermute(lax.slice_in_dim(left, split, None, axis=split_dim), axis, bwd)
            blocks[count // 2] = jnp.concatenate([lo, hi], axis=split_dim)
    return blocks


def in_order(blocks, axis):
    return jnp.roll(jnp.stack(blocks), lax.axis_index(axis), axis=0)


def gather_col(field, y_count, z_count):
    pair = in_order(ring_blocks(field, "y_hi", y_count, 0), "y_hi")
    return ring_blocks(pair, "z", z_count, 0)


def gather_slots(tiles):
    local_slots = tiles.shape[1]
    slot_map = jnp.arange(local_slots, dtype=jnp.int32)
    stride = 1
    stacked = tiles[None]
    for axis in ROW_AXES[::-1]:
        count = lax.axis_size(axis)
        stacked = jnp.stack(ring_blocks(stacked, axis, count, 0)).reshape(-1, *tiles.shape)
        owner = (lax.axis_index(axis) + jnp.arange(count, dtype=jnp.int32)) % count
        slot_map = (owner[:, None] * (stride * local_slots) + slot_map[None, :]).reshape(-1)
        stride = stride * count
    return stacked, slot_map


def place_tiles(dest, tiles, rows):
    positions, block_rows, local_slots, size, _ = tiles.shape
    slots = positions * local_slots

    def kernel(dest_ref, tiles_ref, out_ref):
        out_ref[...] = jnp.zeros(out_ref.shape, out_ref.dtype)
        for b in range(block_rows):
            def place(p, carry):
                target = dest_ref[b * slots + p]

                @pl.when(target >= 0)
                def _():
                    start = pl.multiple_of(target * size, size)
                    out_ref[pl.ds(start, size), b * size:(b + 1) * size] = tiles_ref[p // local_slots, b, p % local_slots]

                return carry

            lax.fori_loop(0, slots, place, 0)

    return pl.pallas_call(
        kernel,
        out_shape=jax.ShapeDtypeStruct((rows * size, block_rows * size), tiles.dtype),
        in_specs=[pl.BlockSpec(memory_space=pltpu.SMEM), pl.BlockSpec(memory_space=pltpu.VMEM)],
        out_specs=pl.BlockSpec(memory_space=pltpu.VMEM),
    )(dest.reshape(-1), tiles)


def body(coeffs, block_tiles, neighbours, density):
    y_count = lax.axis_size("y_hi")
    z_count = lax.axis_size("z")
    local_width = coeffs.shape[1]
    block_rows = neighbours.shape[0]
    slot_count = neighbours.shape[1]
    block_size = block_tiles.shape[2]
    total_blocks = block_rows * y_count * z_count
    col = lax.axis_index("y_hi") * z_count + lax.axis_index("z")
    block_ids = col * block_rows + jnp.arange(block_rows, dtype=jnp.int32)
    region_ids = block_ids // REG_BLK
    region_match = region_ids[:, None] == jnp.arange(density.shape[0], dtype=jnp.int32)[None, :]
    live_counts = jnp.sum(jnp.where(region_match, density[None, :], 0), axis=1)
    live_mask = jnp.arange(slot_count, dtype=jnp.int32)[None, :] < live_counts[:, None]

    tiles, slot_map = gather_slots(jnp.swapaxes(block_tiles, 2, 3))
    ring_neighbours = neighbours[:, slot_map]
    ring_live = live_mask[:, slot_map]
    per_col = block_rows
    owner = ring_neighbours // per_col
    offset = (owner % z_count - lax.axis_index("z")) % z_count
    target = (offset * y_count + owner // z_count) * per_col + ring_neighbours % per_col
    dest = jnp.where(ring_live, target, -1)
    dense = place_tiles(dest, tiles, total_blocks)
    dense = dense.reshape(z_count, y_count, local_width, local_width)

    def apply_hamiltonian(field):
        blocks = gather_col(field, y_count, z_count)
        total = None
        for d, chunk in enumerate(blocks):
            part = jnp.einsum("ymj,yjo->mo", chunk, dense[d], preferred_element_type=jnp.float32)
            total = part if total is None else total + part
        return total

    previous = coeffs
    current = apply_hamiltonian(coeffs).astype(jnp.bfloat16)

    def recurse(repeat, carry):
        previous, current = carry
        product = apply_hamiltonian(current)
        following = (2.0 * product - previous.astype(jnp.float32)).astype(jnp.bfloat16)
        return current, following

    previous, current = lax.fori_loop(0, STEPS - 1, recurse, (previous, current))
    return current


def solution(mesh):
    devices = mesh.devices.reshape(4, 2, 2, 2, 8)
    fine = Mesh(devices, ROW_AXES + COL_AXES)
    placed = (P(ROW_AXES, COL_AXES), P(COL_AXES, ROW_AXES, None, None), P(COL_AXES, None), P())
    return jax.shard_map(
        body, mesh=fine, in_specs=placed, out_specs=P(ROW_AXES, COL_AXES), check_vma=False
    )
```

```python
import jax
import jax.numpy as jnp
from jax import lax
from jax.experimental import pallas as pl
from jax.experimental.pallas import tpu as pltpu
from jax.sharding import Mesh, PartitionSpec as P

STEPS = 3
REG_BLK = 2

ROW_AXES = ("x", "y_lo", "core")
COL_AXES = ("y_hi", "z")


def ring_blocks(piece, axis, count, split_dim):
    fwd = [(i, (i + 1) % count) for i in range(count)]
    bwd = [(i, (i - 1) % count) for i in range(count)]
    blocks = [None] * count
    blocks[0] = piece
    right = piece
    left = piece
    for k in range(1, (count + 1) // 2):
        right = lax.ppermute(right, axis, fwd)
        left = lax.ppermute(left, axis, bwd)
        blocks[(-k) % count] = right
        blocks[k] = left
    if count % 2 == 0 and count > 1:
        if count == 2:
            blocks[1] = lax.ppermute(piece, axis, fwd)
        else:
            split = piece.shape[split_dim] // 2
            lo = lax.ppermute(lax.slice_in_dim(right, 0, split, axis=split_dim), axis, fwd)
            hi = lax.ppermute(lax.slice_in_dim(left, split, None, axis=split_dim), axis, bwd)
            blocks[count // 2] = jnp.concatenate([lo, hi], axis=split_dim)
    return blocks


def in_order(blocks, axis):
    return jnp.roll(jnp.stack(blocks), lax.axis_index(axis), axis=0)


def gather_col(field, y_count, z_count):
    pair = in_order(ring_blocks(field, "y_hi", y_count, 0), "y_hi")
    return ring_blocks(pair, "z", z_count, 0)


def gather_slots(tiles):
    local_slots = tiles.shape[1]
    slot_map = jnp.arange(local_slots, dtype=jnp.int32)
    stride = 1
    stacked = tiles[None]
    for axis in ROW_AXES[::-1]:
        count = lax.axis_size(axis)
        stacked = jnp.stack(ring_blocks(stacked, axis, count, 0)).reshape(-1, *tiles.shape)
        owner = (lax.axis_index(axis) + jnp.arange(count, dtype=jnp.int32)) % count
        slot_map = (owner[:, None] * (stride * local_slots) + slot_map[None, :]).reshape(-1)
        stride = stride * count
    return stacked, slot_map


def place_tiles(dest, tiles, rows):
    positions, block_rows, local_slots, size, _ = tiles.shape
    slots = positions * local_slots

    def kernel(dest_ref, tiles_ref, out_ref):
        out_ref[...] = jnp.zeros(out_ref.shape, out_ref.dtype)
        for b in range(block_rows):
            def place(p, carry):
                target = dest_ref[b * slots + p]

                @pl.when(target >= 0)
                def _():
                    start = pl.multiple_of(target * size, size)
                    out_ref[pl.ds(start, size), b * size:(b + 1) * size] = tiles_ref[p // local_slots, b, p % local_slots]

                return carry

            lax.fori_loop(0, slots, place, 0)

    return pl.pallas_call(
        kernel,
        out_shape=jax.ShapeDtypeStruct((rows * size, block_rows * size), tiles.dtype),
        in_specs=[pl.BlockSpec(memory_space=pltpu.SMEM), pl.BlockSpec(memory_space=pltpu.VMEM)],
        out_specs=pl.BlockSpec(memory_space=pltpu.VMEM),
    )(dest.reshape(-1), tiles)


def body(coeffs, block_tiles, neighbours, density):
    y_count = lax.axis_size("y_hi")
    z_count = lax.axis_size("z")
    local_width = coeffs.shape[1]
    block_rows = neighbours.shape[0]
    slot_count = neighbours.shape[1]
    block_size = block_tiles.shape[2]
    total_blocks = block_rows * y_count * z_count
    col = lax.axis_index("y_hi") * z_count + lax.axis_index("z")
    block_ids = col * block_rows + jnp.arange(block_rows, dtype=jnp.int32)
    region_ids = block_ids // REG_BLK
    region_match = region_ids[:, None] == jnp.arange(density.shape[0], dtype=jnp.int32)[None, :]
    live_counts = jnp.sum(jnp.where(region_match, density[None, :], 0), axis=1)
    live_mask = jnp.arange(slot_count, dtype=jnp.int32)[None, :] < live_counts[:, None]

    tiles, slot_map = gather_slots(jnp.swapaxes(block_tiles, 2, 3))
    ring_neighbours = neighbours[:, slot_map]
    ring_live = live_mask[:, slot_map]
    per_col = block_rows
    owner = ring_neighbours // per_col
    offset = (owner % z_count - lax.axis_index("z")) % z_count
    target = (offset * y_count + owner // z_count) * per_col + ring_neighbours % per_col
    dest = jnp.where(ring_live, target, -1)
    dense = place_tiles(dest, tiles, total_blocks)
    dense = dense.reshape(z_count, y_count, local_width, local_width)

    def apply_hamiltonian(field):
        split = (field.shape[0] * 7 // 16) // 16 * 16
        pairs_first = gather_col(field[:split], y_count, z_count)
        ring_first = ring_blocks(field[split:], "z", z_count, 0)
        pairs_later = [in_order(ring_blocks(block, "y_hi", y_count, 0), "y_hi") for block in ring_first]
        total_first = None
        total_later = None
        for d in range(z_count):
            part = jnp.einsum("ymj,yjo->mo", pairs_first[d], dense[d], preferred_element_type=jnp.float32)
            total_first = part if total_first is None else total_first + part
            part = jnp.einsum("ymj,yjo->mo", pairs_later[d], dense[d], preferred_element_type=jnp.float32)
            total_later = part if total_later is None else total_later + part
        return jnp.concatenate([total_first, total_later], axis=0)

    previous = coeffs
    current = apply_hamiltonian(coeffs).astype(jnp.bfloat16)

    def recurse(repeat, carry):
        previous, current = carry
        product = apply_hamiltonian(current)
        following = (2.0 * product - previous.astype(jnp.float32)).astype(jnp.bfloat16)
        return current, following

    previous, current = lax.fori_loop(0, STEPS - 1, recurse, (previous, current))
    return current


def solution(mesh):
    devices = mesh.devices.reshape(4, 2, 2, 2, 8)
    fine = Mesh(devices, ROW_AXES + COL_AXES)
    placed = (P(ROW_AXES, COL_AXES), P(COL_AXES, ROW_AXES, None, None), P(COL_AXES, None), P())
    return jax.shard_map(
        body, mesh=fine, in_specs=placed, out_specs=P(ROW_AXES, COL_AXES), check_vma=False
    )
```

```python
import jax
import jax.numpy as jnp
from jax import lax
from jax.experimental import pallas as pl
from jax.experimental.pallas import tpu as pltpu
from jax.sharding import Mesh, PartitionSpec as P

STEPS = 3
REG_BLK = 2

ROW_AXES = ("x", "y_lo", "core")
COL_AXES = ("y_hi", "z")


def ring_blocks(piece, axis, count, split_dim):
    fwd = [(i, (i + 1) % count) for i in range(count)]
    bwd = [(i, (i - 1) % count) for i in range(count)]
    blocks = [None] * count
    blocks[0] = piece
    right = piece
    left = piece
    for k in range(1, (count + 1) // 2):
        right = lax.ppermute(right, axis, fwd)
        left = lax.ppermute(left, axis, bwd)
        blocks[(-k) % count] = right
        blocks[k] = left
    if count % 2 == 0 and count > 1:
        if count == 2:
            blocks[1] = lax.ppermute(piece, axis, fwd)
        else:
            split = piece.shape[split_dim] // 2
            lo = lax.ppermute(lax.slice_in_dim(right, 0, split, axis=split_dim), axis, fwd)
            hi = lax.ppermute(lax.slice_in_dim(left, split, None, axis=split_dim), axis, bwd)
            blocks[count // 2] = jnp.concatenate([lo, hi], axis=split_dim)
    return blocks


def in_order(blocks, axis):
    return jnp.roll(jnp.stack(blocks), lax.axis_index(axis), axis=0)


def gather_col(field, y_count, z_count):
    pair = in_order(ring_blocks(field, "y_hi", y_count, 0), "y_hi")
    return ring_blocks(pair, "z", z_count, 0)


def gather_slots(tiles):
    local_slots = tiles.shape[1]
    slot_map = jnp.arange(local_slots, dtype=jnp.int32)
    stride = 1
    stacked = tiles[None]
    for axis in ROW_AXES[::-1]:
        count = lax.axis_size(axis)
        stacked = jnp.stack(ring_blocks(stacked, axis, count, 0)).reshape(-1, *tiles.shape)
        owner = (lax.axis_index(axis) + jnp.arange(count, dtype=jnp.int32)) % count
        slot_map = (owner[:, None] * (stride * local_slots) + slot_map[None, :]).reshape(-1)
        stride = stride * count
    return stacked, slot_map


def place_tiles(dest, tiles, rows):
    positions, block_rows, local_slots, size, _ = tiles.shape
    slots = positions * local_slots

    def kernel(dest_ref, tiles_ref, out_ref):
        out_ref[...] = jnp.zeros(out_ref.shape, out_ref.dtype)
        for b in range(block_rows):
            def place(p, carry):
                target = dest_ref[b * slots + p]

                @pl.when(target >= 0)
                def _():
                    start = pl.multiple_of(target * size, size)
                    out_ref[pl.ds(start, size), b * size:(b + 1) * size] = tiles_ref[p // local_slots, b, p % local_slots]

                return carry

            lax.fori_loop(0, slots, place, 0)

    return pl.pallas_call(
        kernel,
        out_shape=jax.ShapeDtypeStruct((rows * size, block_rows * size), tiles.dtype),
        in_specs=[pl.BlockSpec(memory_space=pltpu.SMEM), pl.BlockSpec(memory_space=pltpu.VMEM)],
        out_specs=pl.BlockSpec(memory_space=pltpu.VMEM),
    )(dest.reshape(-1), tiles)


def body(coeffs, block_tiles, neighbours, density):
    y_count = lax.axis_size("y_hi")
    z_count = lax.axis_size("z")
    local_width = coeffs.shape[1]
    block_rows = neighbours.shape[0]
    slot_count = neighbours.shape[1]
    block_size = block_tiles.shape[2]
    total_blocks = block_rows * y_count * z_count
    col = lax.axis_index("y_hi") * z_count + lax.axis_index("z")
    block_ids = col * block_rows + jnp.arange(block_rows, dtype=jnp.int32)
    region_ids = block_ids // REG_BLK
    region_match = region_ids[:, None] == jnp.arange(density.shape[0], dtype=jnp.int32)[None, :]
    live_counts = jnp.sum(jnp.where(region_match, density[None, :], 0), axis=1)
    live_mask = jnp.arange(slot_count, dtype=jnp.int32)[None, :] < live_counts[:, None]

    tiles = lax.all_gather(jnp.swapaxes(block_tiles, 2, 3), ROW_AXES, axis=1, tiled=True)[None]
    ring_neighbours = neighbours
    ring_live = live_mask
    per_col = block_rows
    owner = ring_neighbours // per_col
    offset = (owner % z_count - lax.axis_index("z")) % z_count
    target = (offset * y_count + owner // z_count) * per_col + ring_neighbours % per_col
    dest = jnp.where(ring_live, target, -1)
    dense = place_tiles(dest, tiles, total_blocks)
    dense = dense.reshape(z_count, y_count, local_width, local_width)

    def apply_hamiltonian(field):
        blocks = gather_col(field, y_count, z_count)
        total = None
        for d, chunk in enumerate(blocks):
            part = jnp.einsum("ymj,yjo->mo", chunk, dense[d], preferred_element_type=jnp.float32)
            total = part if total is None else total + part
        return total

    previous = coeffs
    current = apply_hamiltonian(coeffs).astype(jnp.bfloat16)

    def recurse(repeat, carry):
        previous, current = carry
        product = apply_hamiltonian(current)
        following = (2.0 * product - previous.astype(jnp.float32)).astype(jnp.bfloat16)
        return current, following

    previous, current = lax.fori_loop(0, STEPS - 1, recurse, (previous, current))
    return current


def solution(mesh):
    devices = mesh.devices.reshape(4, 2, 2, 2, 8)
    fine = Mesh(devices, ROW_AXES + COL_AXES)
    placed = (P(ROW_AXES, COL_AXES), P(COL_AXES, ROW_AXES, None, None), P(COL_AXES, None), P())
    return jax.shard_map(
        body, mesh=fine, in_specs=placed, out_specs=P(ROW_AXES, COL_AXES), check_vma=False
    )
```

```python
import jax
import jax.numpy as jnp
from jax import lax
from jax.experimental import pallas as pl
from jax.experimental.pallas import tpu as pltpu
from jax.sharding import Mesh, PartitionSpec as P

STEPS = 3
REG_BLK = 2

ROW_AXES = ("x", "y_lo", "core")
COL_AXES = ("y_hi", "z")


def ring_blocks(piece, axis, count, split_dim):
    fwd = [(i, (i + 1) % count) for i in range(count)]
    bwd = [(i, (i - 1) % count) for i in range(count)]
    blocks = [None] * count
    blocks[0] = piece
    right = piece
    left = piece
    for k in range(1, (count + 1) // 2):
        right = lax.ppermute(right, axis, fwd)
        left = lax.ppermute(left, axis, bwd)
        blocks[(-k) % count] = right
        blocks[k] = left
    if count % 2 == 0 and count > 1:
        if count == 2:
            blocks[1] = lax.ppermute(piece, axis, fwd)
        else:
            split = piece.shape[split_dim] // 2
            lo = lax.ppermute(lax.slice_in_dim(right, 0, split, axis=split_dim), axis, fwd)
            hi = lax.ppermute(lax.slice_in_dim(left, split, None, axis=split_dim), axis, bwd)
            blocks[count // 2] = jnp.concatenate([lo, hi], axis=split_dim)
    return blocks


def in_order(blocks, axis):
    return jnp.roll(jnp.stack(blocks), lax.axis_index(axis), axis=0)


def gather_col(field, y_count, z_count):
    pair = in_order(ring_blocks(field, "y_hi", y_count, 0), "y_hi")
    return ring_blocks(pair, "z", z_count, 0)


def gather_slots(tiles):
    local_slots = tiles.shape[1]
    slot_map = jnp.arange(local_slots, dtype=jnp.int32)
    stride = 1
    stacked = tiles[None]
    for axis in ROW_AXES[::-1]:
        count = lax.axis_size(axis)
        stacked = jnp.stack(ring_blocks(stacked, axis, count, 0)).reshape(-1, *tiles.shape)
        owner = (lax.axis_index(axis) + jnp.arange(count, dtype=jnp.int32)) % count
        slot_map = (owner[:, None] * (stride * local_slots) + slot_map[None, :]).reshape(-1)
        stride = stride * count
    return stacked, slot_map


def place_tiles(dest, tiles, rows):
    positions, block_rows, local_slots, size, _ = tiles.shape
    slots = positions * local_slots

    def kernel(dest_ref, tiles_ref, out_ref):
        out_ref[...] = jnp.zeros(out_ref.shape, out_ref.dtype)
        for b in range(block_rows):
            def place(p, carry):
                target = dest_ref[b * slots + p]

                @pl.when(target >= 0)
                def _():
                    start = pl.multiple_of(target * size, size)
                    out_ref[pl.ds(start, size), b * size:(b + 1) * size] = tiles_ref[p // local_slots, b, p % local_slots]

                return carry

            lax.fori_loop(0, slots, place, 0, unroll=True)

    return pl.pallas_call(
        kernel,
        out_shape=jax.ShapeDtypeStruct((rows * size, block_rows * size), tiles.dtype),
        in_specs=[pl.BlockSpec(memory_space=pltpu.SMEM), pl.BlockSpec(memory_space=pltpu.VMEM)],
        out_specs=pl.BlockSpec(memory_space=pltpu.VMEM),
    )(dest.reshape(-1), tiles)


def body(coeffs, block_tiles, neighbours, density):
    y_count = lax.axis_size("y_hi")
    z_count = lax.axis_size("z")
    local_width = coeffs.shape[1]
    block_rows = neighbours.shape[0]
    slot_count = neighbours.shape[1]
    block_size = block_tiles.shape[2]
    total_blocks = block_rows * y_count * z_count
    col = lax.axis_index("y_hi") * z_count + lax.axis_index("z")
    block_ids = col * block_rows + jnp.arange(block_rows, dtype=jnp.int32)
    region_ids = block_ids // REG_BLK
    region_match = region_ids[:, None] == jnp.arange(density.shape[0], dtype=jnp.int32)[None, :]
    live_counts = jnp.sum(jnp.where(region_match, density[None, :], 0), axis=1)
    live_mask = jnp.arange(slot_count, dtype=jnp.int32)[None, :] < live_counts[:, None]

    tiles = lax.all_gather(jnp.swapaxes(block_tiles, 2, 3), ROW_AXES, axis=1, tiled=True)[None]
    ring_neighbours = neighbours
    ring_live = live_mask
    per_col = block_rows
    owner = ring_neighbours // per_col
    offset = (owner % z_count - lax.axis_index("z")) % z_count
    target = (offset * y_count + owner // z_count) * per_col + ring_neighbours % per_col
    dest = jnp.where(ring_live, target, -1)
    dense = place_tiles(dest, tiles, total_blocks)
    dense = dense.reshape(z_count, y_count, local_width, local_width)

    def apply_hamiltonian(field):
        blocks = gather_col(field, y_count, z_count)
        total = None
        for d, chunk in enumerate(blocks):
            part = jnp.einsum("ymj,yjo->mo", chunk, dense[d], preferred_element_type=jnp.float32)
            total = part if total is None else total + part
        return total

    previous = coeffs
    current = apply_hamiltonian(coeffs).astype(jnp.bfloat16)

    def recurse(repeat, carry):
        previous, current = carry
        product = apply_hamiltonian(current)
        following = (2.0 * product - previous.astype(jnp.float32)).astype(jnp.bfloat16)
        return current, following

    previous, current = lax.fori_loop(0, STEPS - 1, recurse, (previous, current))
    return current


def solution(mesh):
    devices = mesh.devices.reshape(4, 2, 2, 2, 8)
    fine = Mesh(devices, ROW_AXES + COL_AXES)
    placed = (P(ROW_AXES, COL_AXES), P(COL_AXES, ROW_AXES, None, None), P(COL_AXES, None), P())
    return jax.shard_map(
        body, mesh=fine, in_specs=placed, out_specs=P(ROW_AXES, COL_AXES), check_vma=False
    )
```

```python
import jax
import jax.numpy as jnp
from jax import lax
from jax.experimental import pallas as pl
from jax.experimental.pallas import tpu as pltpu
from jax.sharding import Mesh, PartitionSpec as P

STEPS = 3
REG_BLK = 2

ROW_AXES = ("x", "y_lo", "core")
COL_AXES = ("y_hi", "z")


def ring_blocks(piece, axis, count, split_dim):
    fwd = [(i, (i + 1) % count) for i in range(count)]
    bwd = [(i, (i - 1) % count) for i in range(count)]
    blocks = [None] * count
    blocks[0] = piece
    right = piece
    left = piece
    for k in range(1, (count + 1) // 2):
        right = lax.ppermute(right, axis, fwd)
        left = lax.ppermute(left, axis, bwd)
        blocks[(-k) % count] = right
        blocks[k] = left
    if count % 2 == 0 and count > 1:
        blocks[count // 2] = lax.ppermute(right, axis, fwd)
    return blocks


def in_order(blocks, axis):
    return jnp.roll(jnp.stack(blocks), lax.axis_index(axis), axis=0)


def gather_col(field, y_count, z_count):
    pair = in_order(ring_blocks(field, "y_hi", y_count, 0), "y_hi")
    return ring_blocks(pair, "z", z_count, 0)


def gather_slots(tiles):
    local_slots = tiles.shape[1]
    slot_map = jnp.arange(local_slots, dtype=jnp.int32)
    stride = 1
    stacked = tiles[None]
    for axis in ROW_AXES[::-1]:
        count = lax.axis_size(axis)
        stacked = jnp.stack(ring_blocks(stacked, axis, count, 0)).reshape(-1, *tiles.shape)
        owner = (lax.axis_index(axis) + jnp.arange(count, dtype=jnp.int32)) % count
        slot_map = (owner[:, None] * (stride * local_slots) + slot_map[None, :]).reshape(-1)
        stride = stride * count
    return stacked, slot_map


def place_tiles(dest, tiles, rows):
    positions, block_rows, local_slots, size, _ = tiles.shape
    slots = positions * local_slots

    def kernel(dest_ref, tiles_ref, out_ref):
        out_ref[...] = jnp.zeros(out_ref.shape, out_ref.dtype)
        for b in range(block_rows):
            def place(p, carry):
                target = dest_ref[b * slots + p]

                @pl.when(target >= 0)
                def _():
                    start = pl.multiple_of(target * size, size)
                    out_ref[pl.ds(start, size), b * size:(b + 1) * size] = tiles_ref[p // local_slots, b, p % local_slots]

                return carry

            lax.fori_loop(0, slots, place, 0)

    return pl.pallas_call(
        kernel,
        out_shape=jax.ShapeDtypeStruct((rows * size, block_rows * size), tiles.dtype),
        in_specs=[pl.BlockSpec(memory_space=pltpu.SMEM), pl.BlockSpec(memory_space=pltpu.VMEM)],
        out_specs=pl.BlockSpec(memory_space=pltpu.VMEM),
    )(dest.reshape(-1), tiles)


def body(coeffs, block_tiles, neighbours, density):
    y_count = lax.axis_size("y_hi")
    z_count = lax.axis_size("z")
    local_width = coeffs.shape[1]
    block_rows = neighbours.shape[0]
    slot_count = neighbours.shape[1]
    block_size = block_tiles.shape[2]
    total_blocks = block_rows * y_count * z_count
    col = lax.axis_index("y_hi") * z_count + lax.axis_index("z")
    block_ids = col * block_rows + jnp.arange(block_rows, dtype=jnp.int32)
    region_ids = block_ids // REG_BLK
    region_match = region_ids[:, None] == jnp.arange(density.shape[0], dtype=jnp.int32)[None, :]
    live_counts = jnp.sum(jnp.where(region_match, density[None, :], 0), axis=1)
    live_mask = jnp.arange(slot_count, dtype=jnp.int32)[None, :] < live_counts[:, None]

    tiles = lax.all_gather(jnp.swapaxes(block_tiles, 2, 3), ROW_AXES, axis=1, tiled=True)[None]
    ring_neighbours = neighbours
    ring_live = live_mask
    per_col = block_rows
    owner = ring_neighbours // per_col
    offset = (owner % z_count - lax.axis_index("z")) % z_count
    target = (offset * y_count + owner // z_count) * per_col + ring_neighbours % per_col
    dest = jnp.where(ring_live, target, -1)
    dense = place_tiles(dest, tiles, total_blocks)
    dense = dense.reshape(z_count, y_count, local_width, local_width)

    def apply_hamiltonian(field):
        blocks = gather_col(field, y_count, z_count)
        total = None
        for d, chunk in enumerate(blocks):
            part = jnp.einsum("ymj,yjo->mo", chunk, dense[d], preferred_element_type=jnp.float32)
            total = part if total is None else total + part
        return total

    previous = coeffs
    current = apply_hamiltonian(coeffs).astype(jnp.bfloat16)

    def recurse(repeat, carry):
        previous, current = carry
        product = apply_hamiltonian(current)
        following = (2.0 * product - previous.astype(jnp.float32)).astype(jnp.bfloat16)
        return current, following

    previous, current = lax.fori_loop(0, STEPS - 1, recurse, (previous, current))
    return current


def solution(mesh):
    devices = mesh.devices.reshape(4, 2, 2, 2, 8)
    fine = Mesh(devices, ROW_AXES + COL_AXES)
    placed = (P(ROW_AXES, COL_AXES), P(COL_AXES, ROW_AXES, None, None), P(COL_AXES, None), P())
    return jax.shard_map(
        body, mesh=fine, in_specs=placed, out_specs=P(ROW_AXES, COL_AXES), check_vma=False
    )
```

```python
import jax
import jax.numpy as jnp
from jax import lax
from jax.experimental import pallas as pl
from jax.experimental.pallas import tpu as pltpu
from jax.sharding import Mesh, PartitionSpec as P

STEPS = 3
REG_BLK = 2

ROW_AXES = ("x", "y_lo", "core")
COL_AXES = ("y_hi", "z")


def ring_blocks(piece, axis, count, split_dim):
    fwd = [(i, (i + 1) % count) for i in range(count)]
    bwd = [(i, (i - 1) % count) for i in range(count)]
    blocks = [None] * count
    blocks[0] = piece
    right = piece
    left = piece
    for k in range(1, (count + 1) // 2):
        right = lax.ppermute(right, axis, fwd)
        left = lax.ppermute(left, axis, bwd)
        blocks[(-k) % count] = right
        blocks[k] = left
    if count % 2 == 0 and count > 1:
        if count == 2:
            blocks[1] = lax.ppermute(piece, axis, fwd)
        else:
            split = piece.shape[split_dim] // 2
            lo = lax.ppermute(lax.slice_in_dim(right, 0, split, axis=split_dim), axis, fwd)
            hi = lax.ppermute(lax.slice_in_dim(left, split, None, axis=split_dim), axis, bwd)
            blocks[count // 2] = jnp.concatenate([lo, hi], axis=split_dim)
    return blocks


def in_order(blocks, axis):
    return jnp.roll(jnp.stack(blocks), lax.axis_index(axis), axis=0)


def gather_col(field, y_count, z_count):
    pair = in_order(ring_blocks(field, "y_hi", y_count, 0), "y_hi")
    return ring_blocks(pair, "z", z_count, 0)


def gather_slots(tiles):
    local_slots = tiles.shape[1]
    slot_map = jnp.arange(local_slots, dtype=jnp.int32)
    stride = 1
    stacked = tiles[None]
    for axis in ROW_AXES[::-1]:
        count = lax.axis_size(axis)
        stacked = jnp.stack(ring_blocks(stacked, axis, count, 0)).reshape(-1, *tiles.shape)
        owner = (lax.axis_index(axis) + jnp.arange(count, dtype=jnp.int32)) % count
        slot_map = (owner[:, None] * (stride * local_slots) + slot_map[None, :]).reshape(-1)
        stride = stride * count
    return stacked, slot_map


def place_tiles(dest, tiles, rows):
    positions, block_rows, local_slots, size, _ = tiles.shape
    slots = positions * local_slots

    def kernel(dest_ref, tiles_ref, out_ref):
        out_ref[...] = jnp.zeros(out_ref.shape, out_ref.dtype)
        for b in range(block_rows):
            def place(p, carry):
                target = dest_ref[b * slots + p]

                @pl.when(target >= 0)
                def _():
                    start = pl.multiple_of(target * size, size)
                    out_ref[pl.ds(start, size), b * size:(b + 1) * size] = tiles_ref[p // local_slots, b, p % local_slots]

                return carry

            lax.fori_loop(0, slots, place, 0)

    return pl.pallas_call(
        kernel,
        out_shape=jax.ShapeDtypeStruct((rows * size, block_rows * size), tiles.dtype),
        in_specs=[pl.BlockSpec(memory_space=pltpu.SMEM), pl.BlockSpec(memory_space=pltpu.VMEM)],
        out_specs=pl.BlockSpec(memory_space=pltpu.VMEM),
    )(dest.reshape(-1), tiles)


def body(coeffs, block_tiles, neighbours, density):
    y_count = lax.axis_size("y_hi")
    z_count = lax.axis_size("z")
    local_width = coeffs.shape[1]
    block_rows = neighbours.shape[0]
    slot_count = neighbours.shape[1]
    block_size = block_tiles.shape[2]
    total_blocks = block_rows * y_count * z_count
    col = lax.axis_index("y_hi") * z_count + lax.axis_index("z")
    block_ids = col * block_rows + jnp.arange(block_rows, dtype=jnp.int32)
    region_ids = block_ids // REG_BLK
    region_match = region_ids[:, None] == jnp.arange(density.shape[0], dtype=jnp.int32)[None, :]
    live_counts = jnp.sum(jnp.where(region_match, density[None, :], 0), axis=1)
    live_mask = jnp.arange(slot_count, dtype=jnp.int32)[None, :] < live_counts[:, None]

    tiles_t = jnp.swapaxes(block_tiles, 2, 3)
    per_col = block_rows
    owner = neighbours // per_col
    offset = (owner % z_count - lax.axis_index("z")) % z_count
    target = (offset * y_count + owner // z_count) * per_col + neighbours % per_col
    dest = jnp.where(live_mask, target, -1)
    half = block_rows // 2
    denses = []
    for lo, hi in ((0, half), (half, block_rows)):
        tiles = lax.all_gather(tiles_t[lo:hi], ROW_AXES, axis=1, tiled=True)[None]
        dense = place_tiles(dest[lo:hi], tiles, total_blocks)
        denses.append(dense.reshape(z_count, y_count, local_width, (hi - lo) * block_size))

    def apply_hamiltonian(field):
        blocks = gather_col(field, y_count, z_count)
        totals = []
        for dense in denses:
            total = None
            for d, chunk in enumerate(blocks):
                part = jnp.einsum("ymj,yjo->mo", chunk, dense[d], preferred_element_type=jnp.float32)
                total = part if total is None else total + part
            totals.append(total)
        return jnp.concatenate(totals, axis=1)

    previous = coeffs
    current = apply_hamiltonian(coeffs).astype(jnp.bfloat16)

    def recurse(repeat, carry):
        previous, current = carry
        product = apply_hamiltonian(current)
        following = (2.0 * product - previous.astype(jnp.float32)).astype(jnp.bfloat16)
        return current, following

    previous, current = lax.fori_loop(0, STEPS - 1, recurse, (previous, current))
    return current


def solution(mesh):
    devices = mesh.devices.reshape(4, 2, 2, 2, 8)
    fine = Mesh(devices, ROW_AXES + COL_AXES)
    placed = (P(ROW_AXES, COL_AXES), P(COL_AXES, ROW_AXES, None, None), P(COL_AXES, None), P())
    return jax.shard_map(
        body, mesh=fine, in_specs=placed, out_specs=P(ROW_AXES, COL_AXES), check_vma=False
    )
```

```python
import jax
import jax.numpy as jnp
from jax import lax
from jax.experimental import pallas as pl
from jax.experimental.pallas import tpu as pltpu
from jax.sharding import Mesh, PartitionSpec as P

STEPS = 3
REG_BLK = 2

ROW_AXES = ("x", "y_lo", "core")
COL_AXES = ("y_hi", "z")


def ring_blocks(piece, axis, count, split_dim):
    fwd = [(i, (i + 1) % count) for i in range(count)]
    bwd = [(i, (i - 1) % count) for i in range(count)]
    blocks = [None] * count
    blocks[0] = piece
    right = piece
    left = piece
    for k in range(1, (count + 1) // 2):
        right = lax.ppermute(right, axis, fwd)
        left = lax.ppermute(left, axis, bwd)
        blocks[(-k) % count] = right
        blocks[k] = left
    if count % 2 == 0 and count > 1:
        if count == 2:
            blocks[1] = lax.ppermute(piece, axis, fwd)
        else:
            split = piece.shape[split_dim] // 2
            lo = lax.ppermute(lax.slice_in_dim(right, 0, split, axis=split_dim), axis, fwd)
            hi = lax.ppermute(lax.slice_in_dim(left, split, None, axis=split_dim), axis, bwd)
            blocks[count // 2] = jnp.concatenate([lo, hi], axis=split_dim)
    return blocks


def in_order(blocks, axis):
    return jnp.roll(jnp.stack(blocks), lax.axis_index(axis), axis=0)


def gather_col(field, y_count, z_count):
    pair = in_order(ring_blocks(field, "y_hi", y_count, 0), "y_hi")
    return ring_blocks(pair, "z", z_count, 0)


def gather_slots(tiles):
    local_slots = tiles.shape[1]
    slot_map = jnp.arange(local_slots, dtype=jnp.int32)
    stride = 1
    stacked = tiles[None]
    for axis in ROW_AXES[::-1]:
        count = lax.axis_size(axis)
        stacked = jnp.stack(ring_blocks(stacked, axis, count, 0)).reshape(-1, *tiles.shape)
        owner = (lax.axis_index(axis) + jnp.arange(count, dtype=jnp.int32)) % count
        slot_map = (owner[:, None] * (stride * local_slots) + slot_map[None, :]).reshape(-1)
        stride = stride * count
    return stacked, slot_map


def place_tiles(dest, tiles, rows):
    positions, block_rows, local_slots, size, _ = tiles.shape
    slots = positions * local_slots
    group = max(1, 128 // size)

    def kernel(dest_ref, tiles_ref, out_ref):
        first = pl.program_id(0) * group
        out_ref[...] = jnp.zeros(out_ref.shape, out_ref.dtype)
        for b in range(group):
            def place(p, carry):
                target = dest_ref[(first + b) * slots + p]

                @pl.when(target >= 0)
                def _():
                    start = pl.multiple_of(target * size, size)
                    out_ref[pl.ds(start, size), b * size:(b + 1) * size] = tiles_ref[p // local_slots, b, p % local_slots]

                return carry

            lax.fori_loop(0, slots, place, 0)

    return pl.pallas_call(
        kernel,
        grid=(block_rows // group,),
        out_shape=jax.ShapeDtypeStruct((rows * size, block_rows * size), tiles.dtype),
        in_specs=[
            pl.BlockSpec(memory_space=pltpu.SMEM),
            pl.BlockSpec((positions, group, local_slots, size, size), lambda g: (0, g, 0, 0, 0)),
        ],
        out_specs=pl.BlockSpec((rows * size, group * size), lambda g: (0, g)),
    )(dest.reshape(-1), tiles)


def body(coeffs, block_tiles, neighbours, density):
    y_count = lax.axis_size("y_hi")
    z_count = lax.axis_size("z")
    local_width = coeffs.shape[1]
    block_rows = neighbours.shape[0]
    slot_count = neighbours.shape[1]
    block_size = block_tiles.shape[2]
    total_blocks = block_rows * y_count * z_count
    col = lax.axis_index("y_hi") * z_count + lax.axis_index("z")
    block_ids = col * block_rows + jnp.arange(block_rows, dtype=jnp.int32)
    region_ids = block_ids // REG_BLK
    region_match = region_ids[:, None] == jnp.arange(density.shape[0], dtype=jnp.int32)[None, :]
    live_counts = jnp.sum(jnp.where(region_match, density[None, :], 0), axis=1)
    live_mask = jnp.arange(slot_count, dtype=jnp.int32)[None, :] < live_counts[:, None]

    tiles = lax.all_gather(jnp.swapaxes(block_tiles, 2, 3), ROW_AXES, axis=1, tiled=True)[None]
    ring_neighbours = neighbours
    ring_live = live_mask
    per_col = block_rows
    owner = ring_neighbours // per_col
    offset = (owner % z_count - lax.axis_index("z")) % z_count
    target = (offset * y_count + owner // z_count) * per_col + ring_neighbours % per_col
    dest = jnp.where(ring_live, target, -1)
    dense = place_tiles(dest, tiles, total_blocks)
    dense = dense.reshape(z_count, y_count, local_width, local_width)

    def apply_hamiltonian(field):
        blocks = gather_col(field, y_count, z_count)
        total = None
        for d, chunk in enumerate(blocks):
            part = jnp.einsum("ymj,yjo->mo", chunk, dense[d], preferred_element_type=jnp.float32)
            total = part if total is None else total + part
        return total

    previous = coeffs
    current = apply_hamiltonian(coeffs).astype(jnp.bfloat16)

    def recurse(repeat, carry):
        previous, current = carry
        product = apply_hamiltonian(current)
        following = (2.0 * product - previous.astype(jnp.float32)).astype(jnp.bfloat16)
        return current, following

    previous, current = lax.fori_loop(0, STEPS - 1, recurse, (previous, current))
    return current


def solution(mesh):
    devices = mesh.devices.reshape(4, 2, 2, 2, 8)
    fine = Mesh(devices, ROW_AXES + COL_AXES)
    placed = (P(ROW_AXES, COL_AXES), P(COL_AXES, ROW_AXES, None, None), P(COL_AXES, None), P())
    return jax.shard_map(
        body, mesh=fine, in_specs=placed, out_specs=P(ROW_AXES, COL_AXES), check_vma=False
    )
```

```python
import jax
import jax.numpy as jnp
from jax import lax
from jax.experimental import pallas as pl
from jax.experimental.pallas import tpu as pltpu
from jax.sharding import Mesh, PartitionSpec as P

STEPS = 3
REG_BLK = 2

ROW_AXES = ("x", "y_lo", "core")
COL_AXES = ("y_hi", "z")


def ring_blocks(piece, axis, count, split_dim):
    fwd = [(i, (i + 1) % count) for i in range(count)]
    bwd = [(i, (i - 1) % count) for i in range(count)]
    blocks = [None] * count
    blocks[0] = piece
    right = piece
    left = piece
    for k in range(1, (count + 1) // 2):
        right = lax.ppermute(right, axis, fwd)
        left = lax.ppermute(left, axis, bwd)
        blocks[(-k) % count] = right
        blocks[k] = left
    if count % 2 == 0 and count > 1:
        if count == 2:
            blocks[1] = lax.ppermute(piece, axis, fwd)
        else:
            split = piece.shape[split_dim] // 2
            lo = lax.ppermute(lax.slice_in_dim(right, 0, split, axis=split_dim), axis, fwd)
            hi = lax.ppermute(lax.slice_in_dim(left, split, None, axis=split_dim), axis, bwd)
            blocks[count // 2] = jnp.concatenate([lo, hi], axis=split_dim)
    return blocks


def in_order(blocks, axis):
    return jnp.roll(jnp.stack(blocks), lax.axis_index(axis), axis=0)


def gather_col(field, y_count, z_count):
    pair = in_order(ring_blocks(field, "y_hi", y_count, 0), "y_hi")
    return ring_blocks(pair, "z", z_count, 0)


def gather_slots(tiles):
    local_slots = tiles.shape[1]
    slot_map = jnp.arange(local_slots, dtype=jnp.int32)
    stride = 1
    stacked = tiles[None]
    for axis in ROW_AXES[::-1]:
        count = lax.axis_size(axis)
        stacked = jnp.stack(ring_blocks(stacked, axis, count, 0)).reshape(-1, *tiles.shape)
        owner = (lax.axis_index(axis) + jnp.arange(count, dtype=jnp.int32)) % count
        slot_map = (owner[:, None] * (stride * local_slots) + slot_map[None, :]).reshape(-1)
        stride = stride * count
    return stacked, slot_map


def place_tiles(dest, tiles, rows):
    positions, block_rows, local_slots, size, _ = tiles.shape
    slots = positions * local_slots

    def kernel(dest_ref, tiles_ref, out_ref):
        out_ref[...] = jnp.zeros(out_ref.shape, out_ref.dtype)
        for b in range(block_rows):
            def place(p, carry):
                target = dest_ref[b * slots + p]

                @pl.when(target >= 0)
                def _():
                    start = pl.multiple_of(target * size, size)
                    out_ref[pl.ds(start, size), b * size:(b + 1) * size] = tiles_ref[p // local_slots, b, p % local_slots]

                return carry

            lax.fori_loop(0, slots, place, 0)

    return pl.pallas_call(
        kernel,
        out_shape=jax.ShapeDtypeStruct((rows * size, block_rows * size), tiles.dtype),
        in_specs=[pl.BlockSpec(memory_space=pltpu.SMEM), pl.BlockSpec(memory_space=pltpu.VMEM)],
        out_specs=pl.BlockSpec(memory_space=pltpu.VMEM),
    )(dest.reshape(-1), tiles)


def body(coeffs, block_tiles, neighbours, density):
    y_count = lax.axis_size("y_hi")
    z_count = lax.axis_size("z")
    local_width = coeffs.shape[1]
    block_rows = neighbours.shape[0]
    slot_count = neighbours.shape[1]
    block_size = block_tiles.shape[2]
    total_blocks = block_rows * y_count * z_count
    col = lax.axis_index("y_hi") * z_count + lax.axis_index("z")
    block_ids = col * block_rows + jnp.arange(block_rows, dtype=jnp.int32)
    region_ids = block_ids // REG_BLK
    region_match = region_ids[:, None] == jnp.arange(density.shape[0], dtype=jnp.int32)[None, :]
    live_counts = jnp.sum(jnp.where(region_match, density[None, :], 0), axis=1)
    live_mask = jnp.arange(slot_count, dtype=jnp.int32)[None, :] < live_counts[:, None]

    tiles = lax.all_gather(jnp.swapaxes(block_tiles, 2, 3), ROW_AXES, axis=1, tiled=True)[None]
    ring_neighbours = neighbours
    ring_live = live_mask
    per_col = block_rows
    owner = ring_neighbours // per_col
    offset = (owner % z_count - lax.axis_index("z")) % z_count
    target = (offset * y_count + owner // z_count) * per_col + ring_neighbours % per_col
    dest = jnp.where(ring_live, target, -1)
    dense = place_tiles(dest, tiles, total_blocks)
    dense = dense.reshape(z_count, y_count, local_width, local_width)

    def products(pairs, operators):
        totals = []
        for operator in operators:
            total = None
            for d, chunk in enumerate(ring_blocks(pairs, "z", z_count, 0)):
                part = jnp.einsum("ymj,yjo->mo", chunk, operator[d], preferred_element_type=jnp.float32)
                total = part if total is None else total + part
            totals.append(total)
        return totals

    y = lax.axis_index("y_hi")
    swap = [(i, (i + 1) % y_count) for i in range(y_count)]

    def order(own, other):
        return jnp.where(y == 0, jnp.stack([own, other]), jnp.stack([other, own]))

    partner_dense = lax.ppermute(dense, "y_hi", swap)
    previous = coeffs
    partner_previous = lax.ppermute(coeffs, "y_hi", swap)
    (product,) = products(order(coeffs, partner_previous), (dense,))
    current = product.astype(jnp.bfloat16)
    partner_current = lax.ppermute(current, "y_hi", swap)
    own_product, partner_product = products(order(current, partner_current), (dense, partner_dense))
    following = (2.0 * own_product - previous.astype(jnp.float32)).astype(jnp.bfloat16)
    partner_following = (2.0 * partner_product - partner_previous.astype(jnp.float32)).astype(jnp.bfloat16)
    (product,) = products(order(following, partner_following), (dense,))
    return (2.0 * product - current.astype(jnp.float32)).astype(jnp.bfloat16)


def solution(mesh):
    devices = mesh.devices.reshape(4, 2, 2, 2, 8)
    fine = Mesh(devices, ROW_AXES + COL_AXES)
    placed = (P(ROW_AXES, COL_AXES), P(COL_AXES, ROW_AXES, None, None), P(COL_AXES, None), P())
    return jax.shard_map(
        body, mesh=fine, in_specs=placed, out_specs=P(ROW_AXES, COL_AXES), check_vma=False
    )
```

```python
import jax
import jax.numpy as jnp
from jax import lax
from jax.experimental import pallas as pl
from jax.experimental.pallas import tpu as pltpu
from jax.sharding import Mesh, PartitionSpec as P

STEPS = 3
REG_BLK = 2

ROW_AXES = ("x", "y_lo", "core")
COL_AXES = ("y_hi", "z")


def ring_blocks(piece, axis, count, split_dim):
    fwd = [(i, (i + 1) % count) for i in range(count)]
    bwd = [(i, (i - 1) % count) for i in range(count)]
    blocks = [None] * count
    blocks[0] = piece
    right = piece
    left = piece
    for k in range(1, (count + 1) // 2):
        right = lax.ppermute(right, axis, fwd)
        left = lax.ppermute(left, axis, bwd)
        blocks[(-k) % count] = right
        blocks[k] = left
    if count % 2 == 0 and count > 1:
        if count == 2:
            blocks[1] = lax.ppermute(piece, axis, fwd)
        else:
            split = piece.shape[split_dim] // 2
            lo = lax.ppermute(lax.slice_in_dim(right, 0, split, axis=split_dim), axis, fwd)
            hi = lax.ppermute(lax.slice_in_dim(left, split, None, axis=split_dim), axis, bwd)
            blocks[count // 2] = jnp.concatenate([lo, hi], axis=split_dim)
    return blocks


def in_order(blocks, axis):
    return jnp.roll(jnp.stack(blocks), lax.axis_index(axis), axis=0)


def gather_col(field, y_count, z_count):
    pair = in_order(ring_blocks(field, "y_hi", y_count, 0), "y_hi")
    return ring_blocks(pair, "z", z_count, 0)


def gather_slots(tiles):
    local_slots = tiles.shape[1]
    slot_map = jnp.arange(local_slots, dtype=jnp.int32)
    stride = 1
    stacked = tiles[None]
    for axis in ROW_AXES[::-1]:
        count = lax.axis_size(axis)
        stacked = jnp.stack(ring_blocks(stacked, axis, count, 0)).reshape(-1, *tiles.shape)
        owner = (lax.axis_index(axis) + jnp.arange(count, dtype=jnp.int32)) % count
        slot_map = (owner[:, None] * (stride * local_slots) + slot_map[None, :]).reshape(-1)
        stride = stride * count
    return stacked, slot_map


def place_tiles(dest, tiles, rows):
    positions, block_rows, local_slots, size, _ = tiles.shape
    slots = positions * local_slots

    def kernel(dest_ref, tiles_ref, out_ref):
        out_ref[...] = jnp.zeros(out_ref.shape, out_ref.dtype)
        for b in range(block_rows):
            def place(p, carry):
                target = dest_ref[b * slots + p]

                @pl.when(target >= 0)
                def _():
                    start = pl.multiple_of(target * size, size)
                    tile = tiles_ref[p // local_slots, b, p % local_slots].astype(jnp.float32)
                    out_ref[pl.ds(start, size), b * size:(b + 1) * size] = tile.T.astype(out_ref.dtype)

                return carry

            lax.fori_loop(0, slots, place, 0)

    return pl.pallas_call(
        kernel,
        out_shape=jax.ShapeDtypeStruct((rows * size, block_rows * size), tiles.dtype),
        in_specs=[pl.BlockSpec(memory_space=pltpu.SMEM), pl.BlockSpec(memory_space=pltpu.VMEM)],
        out_specs=pl.BlockSpec(memory_space=pltpu.VMEM),
    )(dest.reshape(-1), tiles)


def body(coeffs, block_tiles, neighbours, density):
    y_count = lax.axis_size("y_hi")
    z_count = lax.axis_size("z")
    local_width = coeffs.shape[1]
    block_rows = neighbours.shape[0]
    slot_count = neighbours.shape[1]
    block_size = block_tiles.shape[2]
    total_blocks = block_rows * y_count * z_count
    col = lax.axis_index("y_hi") * z_count + lax.axis_index("z")
    block_ids = col * block_rows + jnp.arange(block_rows, dtype=jnp.int32)
    region_ids = block_ids // REG_BLK
    region_match = region_ids[:, None] == jnp.arange(density.shape[0], dtype=jnp.int32)[None, :]
    live_counts = jnp.sum(jnp.where(region_match, density[None, :], 0), axis=1)
    live_mask = jnp.arange(slot_count, dtype=jnp.int32)[None, :] < live_counts[:, None]

    tiles = lax.all_gather(block_tiles, ROW_AXES, axis=1, tiled=True)[None]
    ring_neighbours = neighbours
    ring_live = live_mask
    per_col = block_rows
    owner = ring_neighbours // per_col
    offset = (owner % z_count - lax.axis_index("z")) % z_count
    target = (offset * y_count + owner // z_count) * per_col + ring_neighbours % per_col
    dest = jnp.where(ring_live, target, -1)
    dense = place_tiles(dest, tiles, total_blocks)
    dense = dense.reshape(z_count, y_count, local_width, local_width)

    def apply_hamiltonian(field):
        blocks = gather_col(field, y_count, z_count)
        total = None
        for d, chunk in enumerate(blocks):
            part = jnp.einsum("ymj,yjo->mo", chunk, dense[d], preferred_element_type=jnp.float32)
            total = part if total is None else total + part
        return total

    previous = coeffs
    current = apply_hamiltonian(coeffs).astype(jnp.bfloat16)

    def recurse(repeat, carry):
        previous, current = carry
        product = apply_hamiltonian(current)
        following = (2.0 * product - previous.astype(jnp.float32)).astype(jnp.bfloat16)
        return current, following

    previous, current = lax.fori_loop(0, STEPS - 1, recurse, (previous, current))
    return current


def solution(mesh):
    devices = mesh.devices.reshape(4, 2, 2, 2, 8)
    fine = Mesh(devices, ROW_AXES + COL_AXES)
    placed = (P(ROW_AXES, COL_AXES), P(COL_AXES, ROW_AXES, None, None), P(COL_AXES, None), P())
    return jax.shard_map(
        body, mesh=fine, in_specs=placed, out_specs=P(ROW_AXES, COL_AXES), check_vma=False
    )
```

```python
import jax
import jax.numpy as jnp
from jax import lax
from jax.experimental import pallas as pl
from jax.experimental.pallas import tpu as pltpu
from jax.sharding import Mesh, PartitionSpec as P

STEPS = 3
REG_BLK = 2

ROW_AXES = ("x", "y_lo", "core")
COL_AXES = ("y_hi", "z")


def ring_blocks(piece, axis, count, split_dim):
    fwd = [(i, (i + 1) % count) for i in range(count)]
    bwd = [(i, (i - 1) % count) for i in range(count)]
    blocks = [None] * count
    blocks[0] = piece
    right = piece
    left = piece
    for k in range(1, (count + 1) // 2):
        right = lax.ppermute(right, axis, fwd)
        left = lax.ppermute(left, axis, bwd)
        blocks[(-k) % count] = right
        blocks[k] = left
    if count % 2 == 0 and count > 1:
        if count == 2:
            blocks[1] = lax.ppermute(piece, axis, fwd)
        else:
            split = piece.shape[split_dim] // 2
            lo = lax.ppermute(lax.slice_in_dim(right, 0, split, axis=split_dim), axis, fwd)
            hi = lax.ppermute(lax.slice_in_dim(left, split, None, axis=split_dim), axis, bwd)
            blocks[count // 2] = jnp.concatenate([lo, hi], axis=split_dim)
    return blocks


def in_order(blocks, axis):
    return jnp.roll(jnp.stack(blocks), lax.axis_index(axis), axis=0)


def gather_col(field, y_count, z_count):
    pair = in_order(ring_blocks(field, "y_hi", y_count, 0), "y_hi")
    return ring_blocks(pair, "z", z_count, 0)


def gather_slots(tiles):
    local_slots = tiles.shape[1]
    slot_map = jnp.arange(local_slots, dtype=jnp.int32)
    stride = 1
    stacked = tiles[None]
    for axis in ROW_AXES[::-1]:
        count = lax.axis_size(axis)
        stacked = jnp.stack(ring_blocks(stacked, axis, count, 0)).reshape(-1, *tiles.shape)
        owner = (lax.axis_index(axis) + jnp.arange(count, dtype=jnp.int32)) % count
        slot_map = (owner[:, None] * (stride * local_slots) + slot_map[None, :]).reshape(-1)
        stride = stride * count
    return stacked, slot_map


def place_tiles(dest, tiles, rows):
    positions, block_rows, local_slots, size, _ = tiles.shape
    slots = positions * local_slots

    def kernel(dest_ref, tiles_ref, out_ref):
        out_ref[...] = jnp.zeros(out_ref.shape, out_ref.dtype)
        for b in range(block_rows):
            def place(p, carry):
                target = dest_ref[b * slots + p]

                @pl.when(target >= 0)
                def _():
                    start = pl.multiple_of(target * size, size)
                    out_ref[pl.ds(start, size), b * size:(b + 1) * size] = tiles_ref[p // local_slots, b, p % local_slots]

                return carry

            lax.fori_loop(0, slots, place, 0)

    return pl.pallas_call(
        kernel,
        out_shape=jax.ShapeDtypeStruct((rows * size, block_rows * size), tiles.dtype),
        in_specs=[pl.BlockSpec(memory_space=pltpu.SMEM), pl.BlockSpec(memory_space=pltpu.VMEM)],
        out_specs=pl.BlockSpec(memory_space=pltpu.VMEM),
    )(dest.reshape(-1), tiles)


def body(coeffs, block_tiles, neighbours, density):
    y_count = lax.axis_size("y_hi")
    z_count = lax.axis_size("z")
    local_width = coeffs.shape[1]
    block_rows = neighbours.shape[0]
    slot_count = neighbours.shape[1]
    block_size = block_tiles.shape[2]
    total_blocks = block_rows * y_count * z_count
    col = lax.axis_index("y_hi") * z_count + lax.axis_index("z")
    block_ids = col * block_rows + jnp.arange(block_rows, dtype=jnp.int32)
    region_ids = block_ids // REG_BLK
    region_match = region_ids[:, None] == jnp.arange(density.shape[0], dtype=jnp.int32)[None, :]
    live_counts = jnp.sum(jnp.where(region_match, density[None, :], 0), axis=1)
    live_mask = jnp.arange(slot_count, dtype=jnp.int32)[None, :] < live_counts[:, None]

    dense_rows = jnp.swapaxes(block_tiles, 2, 3).reshape(block_tiles.shape[0], block_tiles.shape[1], -1, 128)
    tiles = lax.all_gather(dense_rows, ROW_AXES, axis=1, tiled=True)
    tiles = tiles.reshape(tiles.shape[0], tiles.shape[1], block_tiles.shape[3], block_tiles.shape[2])[None]
    ring_neighbours = neighbours
    ring_live = live_mask
    per_col = block_rows
    owner = ring_neighbours // per_col
    offset = (owner % z_count - lax.axis_index("z")) % z_count
    target = (offset * y_count + owner // z_count) * per_col + ring_neighbours % per_col
    dest = jnp.where(ring_live, target, -1)
    dense = place_tiles(dest, tiles, total_blocks)
    dense = dense.reshape(z_count, y_count, local_width, local_width)

    def apply_hamiltonian(field):
        blocks = gather_col(field, y_count, z_count)
        total = None
        for d, chunk in enumerate(blocks):
            part = jnp.einsum("ymj,yjo->mo", chunk, dense[d], preferred_element_type=jnp.float32)
            total = part if total is None else total + part
        return total

    previous = coeffs
    current = apply_hamiltonian(coeffs).astype(jnp.bfloat16)

    def recurse(repeat, carry):
        previous, current = carry
        product = apply_hamiltonian(current)
        following = (2.0 * product - previous.astype(jnp.float32)).astype(jnp.bfloat16)
        return current, following

    previous, current = lax.fori_loop(0, STEPS - 1, recurse, (previous, current))
    return current


def solution(mesh):
    devices = mesh.devices.reshape(4, 2, 2, 2, 8)
    fine = Mesh(devices, ROW_AXES + COL_AXES)
    placed = (P(ROW_AXES, COL_AXES), P(COL_AXES, ROW_AXES, None, None), P(COL_AXES, None), P())
    return jax.shard_map(
        body, mesh=fine, in_specs=placed, out_specs=P(ROW_AXES, COL_AXES), check_vma=False
    )
```

```python
import jax
import jax.numpy as jnp
from jax import lax
from jax.experimental import pallas as pl
from jax.experimental.pallas import tpu as pltpu
from jax.sharding import Mesh, PartitionSpec as P

STEPS = 3
REG_BLK = 2

ROW_AXES = ("x", "y_lo", "core")
COL_AXES = ("y_hi", "z")


def ring_blocks(piece, axis, count, split_dim):
    fwd = [(i, (i + 1) % count) for i in range(count)]
    bwd = [(i, (i - 1) % count) for i in range(count)]
    blocks = [None] * count
    blocks[0] = piece
    right = piece
    left = piece
    for k in range(1, (count + 1) // 2):
        right = lax.ppermute(right, axis, fwd)
        left = lax.ppermute(left, axis, bwd)
        blocks[(-k) % count] = right
        blocks[k] = left
    if count % 2 == 0 and count > 1:
        if count == 2:
            blocks[1] = lax.ppermute(piece, axis, fwd)
        else:
            split = piece.shape[split_dim] // 2
            lo = lax.ppermute(lax.slice_in_dim(right, 0, split, axis=split_dim), axis, fwd)
            hi = lax.ppermute(lax.slice_in_dim(left, split, None, axis=split_dim), axis, bwd)
            blocks[count // 2] = jnp.concatenate([lo, hi], axis=split_dim)
    return blocks


def in_order(blocks, axis):
    return jnp.roll(jnp.stack(blocks), lax.axis_index(axis), axis=0)


def gather_col(field, y_count, z_count):
    pair = in_order(ring_blocks(field, "y_hi", y_count, 0), "y_hi")
    return ring_blocks(pair, "z", z_count, 0)


def gather_slots(tiles):
    local_slots = tiles.shape[1]
    slot_map = jnp.arange(local_slots, dtype=jnp.int32)
    stride = 1
    stacked = tiles[None]
    for axis in ROW_AXES[::-1]:
        count = lax.axis_size(axis)
        stacked = jnp.stack(ring_blocks(stacked, axis, count, 0)).reshape(-1, *tiles.shape)
        owner = (lax.axis_index(axis) + jnp.arange(count, dtype=jnp.int32)) % count
        slot_map = (owner[:, None] * (stride * local_slots) + slot_map[None, :]).reshape(-1)
        stride = stride * count
    return stacked, slot_map


def place_tiles(dest, tiles, rows):
    positions, block_rows, local_slots, size, _ = tiles.shape
    slots = positions * local_slots

    def kernel(dest_ref, tiles_ref, out_ref):
        out_ref[...] = jnp.zeros(out_ref.shape, out_ref.dtype)
        for b in range(block_rows):
            def place(p, carry):
                target = dest_ref[b * slots + p]
                target = jnp.where(target >= 0, target, rows)
                start = pl.multiple_of(target * size, size)
                out_ref[pl.ds(start, size), b * size:(b + 1) * size] = tiles_ref[p // local_slots, b, p % local_slots]
                return carry

            lax.fori_loop(0, slots, place, 0, unroll=True)

    return pl.pallas_call(
        kernel,
        out_shape=jax.ShapeDtypeStruct(((rows + 1) * size, block_rows * size), tiles.dtype),
        in_specs=[pl.BlockSpec(memory_space=pltpu.SMEM), pl.BlockSpec(memory_space=pltpu.VMEM)],
        out_specs=pl.BlockSpec(memory_space=pltpu.VMEM),
    )(dest.reshape(-1), tiles)


def body(coeffs, block_tiles, neighbours, density):
    y_count = lax.axis_size("y_hi")
    z_count = lax.axis_size("z")
    local_width = coeffs.shape[1]
    block_rows = neighbours.shape[0]
    slot_count = neighbours.shape[1]
    block_size = block_tiles.shape[2]
    total_blocks = block_rows * y_count * z_count
    col = lax.axis_index("y_hi") * z_count + lax.axis_index("z")
    block_ids = col * block_rows + jnp.arange(block_rows, dtype=jnp.int32)
    region_ids = block_ids // REG_BLK
    region_match = region_ids[:, None] == jnp.arange(density.shape[0], dtype=jnp.int32)[None, :]
    live_counts = jnp.sum(jnp.where(region_match, density[None, :], 0), axis=1)
    live_mask = jnp.arange(slot_count, dtype=jnp.int32)[None, :] < live_counts[:, None]

    tiles = lax.all_gather(jnp.swapaxes(block_tiles, 2, 3), ROW_AXES, axis=1, tiled=True)[None]
    ring_neighbours = neighbours
    ring_live = live_mask
    per_col = block_rows
    owner = ring_neighbours // per_col
    offset = (owner % z_count - lax.axis_index("z")) % z_count
    target = (offset * y_count + owner // z_count) * per_col + ring_neighbours % per_col
    dest = jnp.where(ring_live, target, -1)
    dense = place_tiles(dest, tiles, total_blocks)
    dense = dense[: total_blocks * block_size].reshape(z_count, y_count, local_width, local_width)

    def apply_hamiltonian(field):
        blocks = gather_col(field, y_count, z_count)
        total = None
        for d, chunk in enumerate(blocks):
            part = jnp.einsum("ymj,yjo->mo", chunk, dense[d], preferred_element_type=jnp.float32)
            total = part if total is None else total + part
        return total

    previous = coeffs
    current = apply_hamiltonian(coeffs).astype(jnp.bfloat16)

    def recurse(repeat, carry):
        previous, current = carry
        product = apply_hamiltonian(current)
        following = (2.0 * product - previous.astype(jnp.float32)).astype(jnp.bfloat16)
        return current, following

    previous, current = lax.fori_loop(0, STEPS - 1, recurse, (previous, current))
    return current


def solution(mesh):
    devices = mesh.devices.reshape(4, 2, 2, 2, 8)
    fine = Mesh(devices, ROW_AXES + COL_AXES)
    placed = (P(ROW_AXES, COL_AXES), P(COL_AXES, ROW_AXES, None, None), P(COL_AXES, None), P())
    return jax.shard_map(
        body, mesh=fine, in_specs=placed, out_specs=P(ROW_AXES, COL_AXES), check_vma=False
    )
```

```python
import jax
import jax.numpy as jnp
from jax import lax
from jax.experimental import pallas as pl
from jax.experimental.pallas import tpu as pltpu
from jax.sharding import Mesh, PartitionSpec as P

STEPS = 3
REG_BLK = 2

ROW_AXES = ("x", "y_lo", "core")
COL_AXES = ("y_hi", "z")


def ring_blocks(piece, axis, count, split_dim):
    fwd = [(i, (i + 1) % count) for i in range(count)]
    bwd = [(i, (i - 1) % count) for i in range(count)]
    blocks = [None] * count
    blocks[0] = piece
    right = piece
    left = piece
    for k in range(1, (count + 1) // 2):
        right = lax.ppermute(right, axis, fwd)
        left = lax.ppermute(left, axis, bwd)
        blocks[(-k) % count] = right
        blocks[k] = left
    if count % 2 == 0 and count > 1:
        if count == 2:
            blocks[1] = lax.ppermute(piece, axis, fwd)
        else:
            split = piece.shape[split_dim] // 2
            lo = lax.ppermute(lax.slice_in_dim(right, 0, split, axis=split_dim), axis, fwd)
            hi = lax.ppermute(lax.slice_in_dim(left, split, None, axis=split_dim), axis, bwd)
            blocks[count // 2] = jnp.concatenate([lo, hi], axis=split_dim)
    return blocks


def in_order(blocks, axis):
    return jnp.roll(jnp.stack(blocks), lax.axis_index(axis), axis=0)


def gather_col(field, y_count, z_count):
    pair = in_order(ring_blocks(field, "y_hi", y_count, 0), "y_hi")
    return ring_blocks(pair, "z", z_count, 0)


def gather_slots(tiles):
    local_slots = tiles.shape[1]
    slot_map = jnp.arange(local_slots, dtype=jnp.int32)
    stride = 1
    stacked = tiles[None]
    for axis in ROW_AXES[::-1]:
        count = lax.axis_size(axis)
        stacked = jnp.stack(ring_blocks(stacked, axis, count, 0)).reshape(-1, *tiles.shape)
        owner = (lax.axis_index(axis) + jnp.arange(count, dtype=jnp.int32)) % count
        slot_map = (owner[:, None] * (stride * local_slots) + slot_map[None, :]).reshape(-1)
        stride = stride * count
    return stacked, slot_map


def place_tiles(dest, tiles, rows):
    positions, block_rows, local_slots, size, _ = tiles.shape
    slots = positions * local_slots

    def kernel(dest_ref, tiles_ref, out_ref):
        out_ref[...] = jnp.zeros(out_ref.shape, out_ref.dtype)
        for b in range(block_rows):
            def place(p, carry):
                target = dest_ref[b * slots + p]
                target = jnp.where(target >= 0, target, rows)
                start = pl.multiple_of(target * size, size)
                out_ref[pl.ds(start, size), b * size:(b + 1) * size] = tiles_ref[p // local_slots, b, p % local_slots]
                return carry

            lax.fori_loop(0, slots, place, 0, unroll=True)

    return pl.pallas_call(
        kernel,
        out_shape=jax.ShapeDtypeStruct(((rows + 1) * size, block_rows * size), tiles.dtype),
        in_specs=[pl.BlockSpec(memory_space=pltpu.SMEM), pl.BlockSpec(memory_space=pltpu.VMEM)],
        out_specs=pl.BlockSpec(memory_space=pltpu.VMEM),
    )(dest.reshape(-1), tiles)


def body(coeffs, block_tiles, neighbours, density):
    y_count = lax.axis_size("y_hi")
    z_count = lax.axis_size("z")
    local_width = coeffs.shape[1]
    block_rows = neighbours.shape[0]
    slot_count = neighbours.shape[1]
    block_size = block_tiles.shape[2]
    total_blocks = block_rows * y_count * z_count
    col = lax.axis_index("y_hi") * z_count + lax.axis_index("z")
    block_ids = col * block_rows + jnp.arange(block_rows, dtype=jnp.int32)
    region_ids = block_ids // REG_BLK
    region_match = region_ids[:, None] == jnp.arange(density.shape[0], dtype=jnp.int32)[None, :]
    live_counts = jnp.sum(jnp.where(region_match, density[None, :], 0), axis=1)
    live_mask = jnp.arange(slot_count, dtype=jnp.int32)[None, :] < live_counts[:, None]

    tiles = lax.all_gather(jnp.swapaxes(block_tiles, 2, 3), ROW_AXES, axis=1, tiled=True)[None]
    ring_neighbours = neighbours
    ring_live = live_mask
    per_col = block_rows
    owner = ring_neighbours // per_col
    offset = (owner % z_count - lax.axis_index("z")) % z_count
    target = (offset * y_count + owner // z_count) * per_col + ring_neighbours % per_col
    dest = jnp.where(ring_live, target, -1)
    dense = place_tiles(dest, tiles, total_blocks)
    chunk_rows = y_count * local_width

    def apply_hamiltonian(field):
        blocks = gather_col(field, y_count, z_count)
        total = None
        for d, chunk in enumerate(blocks):
            operator = lax.slice_in_dim(dense, d * chunk_rows, (d + 1) * chunk_rows).reshape(y_count, local_width, -1)
            part = jnp.einsum("ymj,yjo->mo", chunk, operator, preferred_element_type=jnp.float32)
            total = part if total is None else total + part
        return total

    previous = coeffs
    current = apply_hamiltonian(coeffs).astype(jnp.bfloat16)

    def recurse(repeat, carry):
        previous, current = carry
        product = apply_hamiltonian(current)
        following = (2.0 * product - previous.astype(jnp.float32)).astype(jnp.bfloat16)
        return current, following

    previous, current = lax.fori_loop(0, STEPS - 1, recurse, (previous, current))
    return current


def solution(mesh):
    devices = mesh.devices.reshape(4, 2, 2, 2, 8)
    fine = Mesh(devices, ROW_AXES + COL_AXES)
    placed = (P(ROW_AXES, COL_AXES), P(COL_AXES, ROW_AXES, None, None), P(COL_AXES, None), P())
    return jax.shard_map(
        body, mesh=fine, in_specs=placed, out_specs=P(ROW_AXES, COL_AXES), check_vma=False
    )
```
